32 devices in a mesh: seq: 4 (over z), ch: 8 (over y, x, core).
Axes of the slice: x: 2, y: 2, z: 4, core: 2. Of those that a mesh axis runs over, the one named last changes fastest.
Arguments:
- inputs: bfloat16 [1024, 8192], P('seq', 'ch'), may hold values from -6 to 6
- w_in: bfloat16 [3, 8192, 8192], P(None, 'seq', 'ch'), may hold values from -0.0625 to 0.0625
- short_filter: float32 [3, 3, 8192], P(None, None, 'ch'), may hold values from -3 to 3
- rates: float32 [16, 8192], P(None, 'ch'), may hold values from 9.765625e-05 to 0.05
- residues: float32 [16, 8192], P(None, 'ch'), may hold values from -3 to 3
- skip: float32 [8192], P('ch'), may hold values from -3 to 3
Outputs:
- gated: bfloat16 [1024, 8192], P('seq', 'ch')
The draws below stay inside these ranges and needn't reach their ends.
All inputs are finite; a program needn't handle non-finite values.
Results may differ from the reference program's by a relative error of at most 0.0065.
Values may be sent and summed in bfloat16 or wider, within the bound.
No kernel may reach another device: no remote copies, remote signals or barrier semaphores. Data moves between devices by JAX's collectives and lax.ppermute only.
A program may use at most 128 MiB of HBM per device.

```python
import math
import jax
import jax.numpy as jnp
from jax import lax

D = 8192
MODES = 16
TAPS = 3
TOKENS = 1024


def block_levels(key, dims, pieces, low, largest):
    gain = 1.0
    for axis_at, parts in pieces:
        draws = jax.random.uniform(jax.random.fold_in(jax.random.fold_in(key, 6), axis_at), (parts,), jnp.float32, low / len(pieces), largest / len(pieces))
        gain = gain * jnp.repeat(jnp.exp(draws), dims[axis_at] // parts).reshape((-1,) + (1,) * (len(dims) - 1 - axis_at))
    return gain


def scatter_about(stream_key, extent, scale, most, split=(), kind=jnp.bfloat16):
    result = scale * jax.random.normal(stream_key, extent, jnp.float32)
    if split:
        result = result * block_levels(stream_key, extent, split, -0.22, 0.18)
    return jnp.clip(result, -most, most).astype(kind)


def setup_inputs(seed: int = 0) -> dict:
    streams_of = jax.random.split(jax.random.key(seed), 7)
    inputs = scatter_about(streams_of[0], (TOKENS, D), 1.0, 6.0, ((0, 4), (1, 8)))
    w_in = scatter_about(streams_of[1], (3, D, D), D ** -0.5, 0.0625, ((1, 4), (2, 8)))
    short_filter = scatter_about(streams_of[2], (3, TAPS, D), 0.6, 3.0, ((2, 8),), jnp.float32)
    rates = jnp.clip(jnp.exp(math.log(0.05) - 6.2383246 * jax.random.uniform(streams_of[3], (MODES, D), jnp.float32) ** block_levels(streams_of[3], (MODES, D), ((1, 8),), -0.2, 0.2)), 9.765625145519152e-05, 0.05)
    residues = scatter_about(streams_of[4], (MODES, D), 0.5, 3.0, ((1, 8),), jnp.float32)
    skip = scatter_about(streams_of[5], (D,), 0.5, 3.0, ((0, 8),), jnp.float32)
    return {"inputs": inputs, "w_in": w_in, "short_filter": short_filter, "rates": rates, "residues": residues, "skip": skip}


def reference(inputs, w_in, short_filter, rates, residues, skip):
    proj = jnp.stack([jnp.dot(inputs, w_in[i], preferred_element_type=jnp.float32).astype(jnp.bfloat16) for i in range(3)])
    padded = jnp.concatenate([jnp.zeros((3, TAPS - 1, D), jnp.bfloat16), proj], axis=1).astype(jnp.float32)
    mixed = jnp.zeros((3, TOKENS, D), jnp.float32)
    for j in range(TAPS):
        mixed = mixed + short_filter[:, j, None, :] * padded[:, TAPS - 1 - j:TAPS - 1 - j + TOKENS, :]
    query, key, value = (mixed[0], mixed[1], mixed[2])
    drive = key * value
    factor = jnp.exp(-rates)
    scaled = residues * jnp.sqrt(1.0 - jnp.exp(-2.0 * rates))

    def advance(state, entry):
        state = factor * state + entry[None, :]
        return (state, lax.optimization_barrier(jnp.sum(scaled * state, axis=0)))
    _, longconv = lax.scan(advance, jnp.zeros((MODES, D), jnp.float32), drive)
    return (query * (longconv + skip[None, :] * drive)).astype(jnp.bfloat16)
```

```python
import jax
import jax.numpy as jnp
from jax import lax
from jax.sharding import PartitionSpec as P

TAPS = 3


def passed_along(block, axis, distance):
    devices = range(lax.axis_size(axis))
    route = [(i - distance, i) for i in devices if i - distance in devices]
    return lax.ppermute(block, axis, route)


def carried_in(part, axis, combine, identity):
    place = lax.axis_index(axis)
    gathered = jax.tree.map(lambda a: lax.all_gather(a, axis), part)
    state = jax.tree.map(lambda a, e: jnp.zeros_like(a) + jnp.asarray(e, a.dtype), part, identity)

    def one(hop, state):
        return combine(
            state, jax.tree.map(lambda a: lax.dynamic_index_in_dim(a, hop, 0, False), gathered)
        )

    return lax.fori_loop(0, place, one, state)


def combine(earlier, later):
    return (earlier[0] * later[0], earlier[1] * later[0] + later[1])


def project(inputs, w_in):
    tok_rows = inputs.shape[0]
    n_seq = lax.axis_size("seq")
    n_ch = lax.axis_size("ch")
    features = lax.all_gather(inputs, "ch", axis=1, tiled=True)
    piece = features.shape[1] // (n_seq * n_ch)
    features = features.reshape(tok_rows, n_seq, n_ch, piece)
    mine = lax.dynamic_index_in_dim(features, lax.axis_index("ch"), 2, False)
    rows = lax.all_to_all(mine, "seq", 1, 0, tiled=True)
    rows = rows.reshape(n_seq * tok_rows, piece)
    block = lax.all_gather(rows, "ch", axis=1, tiled=True)
    partial = jnp.einsum("td,kdc->ktc", block, w_in, preferred_element_type=jnp.float32)
    return lax.psum_scatter(partial, "seq", scatter_dimension=1, tiled=True)


def per_device(inputs, w_in, short_filter, rates, residues, skip):
    tok_rows = inputs.shape[0]
    width = w_in.shape[2]
    modes = rates.shape[0]
    proj = project(inputs, w_in).astype(jnp.bfloat16)
    prior = passed_along(proj[:, tok_rows - (TAPS - 1) :, :], "seq", 1)
    padded = jnp.concatenate([prior, proj], axis=1).astype(jnp.float32)
    mixed = jnp.zeros((3, tok_rows, width), jnp.float32)
    for j in range(TAPS):
        mixed = (
            mixed
            + short_filter[:, j, None, :] * padded[:, TAPS - 1 - j : TAPS - 1 - j + tok_rows, :]
        )
    query, key, value = (mixed[0], mixed[1], mixed[2])
    drive = key * value
    position = jnp.arange(tok_rows, dtype=jnp.float32)
    scaled = residues * jnp.sqrt(1.0 - jnp.exp(-2.0 * rates))
    end_powers = jnp.exp(-rates[None, :, :] * (tok_rows - 1.0 - position)[:, None, None])
    end_state = jnp.sum(end_powers * drive[:, None, :], axis=0)
    block_decay = jnp.exp(-rates * tok_rows)
    identity = (jnp.ones_like(block_decay), jnp.zeros_like(end_state))
    entering = carried_in((block_decay, end_state), "seq", combine, identity)[1]
    start_powers = jnp.exp(-rates[None, :, :] * (position + 1.0)[:, None, None])
    cross = jnp.sum(start_powers * (scaled * entering)[None, :, :], axis=1)
    center = (tok_rows - 1.0) / 2.0
    offset = (position - center)[:, None, None]
    rising = jnp.exp(rates[None, :, :] * offset) * drive[:, None, :]
    offsets = jnp.arange(tok_rows, dtype=jnp.int32)
    lower = (offsets[:, None] >= offsets[None, :]).astype(jnp.float32)
    prefix = jnp.dot(
        lower, rising.reshape(tok_rows, modes * width), precision=lax.Precision.HIGHEST
    )
    prefix = prefix.reshape(tok_rows, modes, width)
    falling = jnp.exp(-rates[None, :, :] * offset) * scaled[None, :, :]
    local = jnp.sum(falling * prefix, axis=1)
    return (query * (local + cross + skip[None, :] * drive)).astype(jnp.bfloat16)


def solution(mesh):
    in_specs = (
        P("seq", "ch"),
        P(None, "seq", "ch"),
        P(None, None, "ch"),
        P(None, "ch"),
        P(None, "ch"),
        P("ch"),
    )
    out_specs = P("seq", "ch")
    return jax.shard_map(
        per_device, mesh=mesh, in_specs=in_specs, out_specs=out_specs, check_vma=False
    )
```

```python
import jax
import jax.numpy as jnp
from jax import lax
from jax.sharding import PartitionSpec as P

TAPS = 3


def passed_along(block, axis, distance):
    devices = range(lax.axis_size(axis))
    route = [(i - distance, i) for i in devices if i - distance in devices]
    return lax.ppermute(block, axis, route)


def carried_in(end_state, decay, axis):
    total = lax.axis_size(axis)
    state = jnp.zeros_like(end_state)
    for distance in range(total - 1, 0, -1):
        state = state * decay + passed_along(end_state, axis, distance)
    return state


def project(inputs, w_in):
    tok_rows, local = inputs.shape
    n_seq = lax.axis_size("seq")
    n_ch = lax.axis_size("ch")
    share = tok_rows // n_ch
    pieces = lax.all_to_all(inputs.reshape(n_ch, share, local), "ch", 0, 0, tiled=True)
    pieces = pieces.transpose(1, 0, 2).reshape(share, n_seq, (n_ch * local) // n_seq)
    rows = lax.all_to_all(pieces, "seq", 1, 0, tiled=True)
    rows = rows.reshape(n_seq, share, rows.shape[-1])
    block = lax.all_gather(rows, "ch", axis=1, tiled=True)
    block = block.reshape(n_seq * tok_rows, block.shape[-1])
    partial = jnp.einsum("td,kdc->ktc", block, w_in, preferred_element_type=jnp.float32)
    return lax.psum_scatter(partial, "seq", scatter_dimension=1, tiled=True)


def per_device(inputs, w_in, short_filter, rates, residues, skip):
    tok_rows = inputs.shape[0]
    width = w_in.shape[2]
    modes = rates.shape[0]
    proj = project(inputs, w_in).astype(jnp.bfloat16)
    prior = passed_along(proj[:, tok_rows - (TAPS - 1) :, :], "seq", 1)
    padded = jnp.concatenate([prior, proj], axis=1).astype(jnp.float32)
    mixed = jnp.zeros((3, tok_rows, width), jnp.float32)
    for j in range(TAPS):
        mixed = (
            mixed
            + short_filter[:, j, None, :] * padded[:, TAPS - 1 - j : TAPS - 1 - j + tok_rows, :]
        )
    query, key, value = (mixed[0], mixed[1], mixed[2])
    drive = key * value
    position = jnp.arange(tok_rows, dtype=jnp.float32)
    scaled = residues * jnp.sqrt(1.0 - jnp.exp(-2.0 * rates))
    end_powers = jnp.exp(-rates[None, :, :] * (tok_rows - 1.0 - position)[:, None, None])
    end_state = jnp.sum(end_powers * drive[:, None, :], axis=0)
    block_decay = jnp.exp(-rates * tok_rows)
    entering = carried_in(end_state, block_decay, "seq")
    start_powers = jnp.exp(-rates[None, :, :] * (position + 1.0)[:, None, None])
    cross = jnp.sum(start_powers * (scaled * entering)[None, :, :], axis=1)
    center = (tok_rows - 1.0) / 2.0
    offset = (position - center)[:, None, None]
    rising = jnp.exp(rates[None, :, :] * offset) * drive[:, None, :]
    offsets = jnp.arange(tok_rows, dtype=jnp.int32)
    lower = (offsets[:, None] >= offsets[None, :]).astype(jnp.float32)
    prefix = jnp.dot(
        lower, rising.reshape(tok_rows, modes * width), precision=lax.Precision.HIGHEST
    )
    prefix = prefix.reshape(tok_rows, modes, width)
    falling = jnp.exp(-rates[None, :, :] * offset) * scaled[None, :, :]
    local = jnp.sum(falling * prefix, axis=1)
    return (query * (local + cross + skip[None, :] * drive)).astype(jnp.bfloat16)


def solution(mesh):
    in_specs = (
        P("seq", "ch"),
        P(None, "seq", "ch"),
        P(None, None, "ch"),
        P(None, "ch"),
        P(None, "ch"),
        P("ch"),
    )
    out_specs = P("seq", "ch")
    return jax.shard_map(
        per_device, mesh=mesh, in_specs=in_specs, out_specs=out_specs, check_vma=False
    )
```

```python
import jax
import jax.numpy as jnp
from jax import lax
from jax.sharding import PartitionSpec as P

TAPS = 3
CHUNKS = 2


def passed_along(block, axis, distance):
    devices = range(lax.axis_size(axis))
    route = [(i - distance, i) for i in devices if i - distance in devices]
    return lax.ppermute(block, axis, route)


def carried_in(end_state, decay, axis):
    total = lax.axis_size(axis)
    state = jnp.zeros_like(end_state)
    for distance in range(total - 1, 0, -1):
        state = state * decay + passed_along(end_state, axis, distance)
    return state


def gather_block(inputs):
    tok_rows, local = inputs.shape
    n_seq = lax.axis_size("seq")
    n_ch = lax.axis_size("ch")
    share = tok_rows // n_ch
    pieces = lax.all_to_all(inputs.reshape(n_ch, share, local), "ch", 0, 0, tiled=True)
    pieces = pieces.transpose(1, 0, 2).reshape(share, n_seq, (n_ch * local) // n_seq)
    rows = lax.all_to_all(pieces, "seq", 1, 0, tiled=True)
    rows = rows.reshape(n_seq, share, rows.shape[-1])
    block = lax.all_gather(rows, "ch", axis=1, tiled=True)
    return block.reshape(n_seq * tok_rows, block.shape[-1])


def project(block, w_in):
    partial = jnp.einsum("td,kdc->ktc", block, w_in, preferred_element_type=jnp.float32)
    return lax.psum_scatter(partial, "seq", scatter_dimension=1, tiled=True)


def per_device(inputs, w_in, short_filter, rates, residues, skip):
    block = gather_block(inputs)
    width = w_in.shape[2]
    chunks = max(1, min(CHUNKS, width // 128))
    step = width // chunks
    parts = [project(block, w_in[:, :, i * step : (i + 1) * step]) for i in range(chunks)]
    outs = []
    for i in range(chunks):
        cols = slice(i * step, (i + 1) * step)
        part = parts[i]
        if outs:
            outs[-1], part = lax.optimization_barrier((outs[-1], part))
        outs.append(
            chunk(part, inputs.shape[0], short_filter[:, :, cols],
                  rates[:, cols], residues[:, cols], skip[cols])
        )
    return jnp.concatenate(outs, axis=1)


def chunk(part, tok_rows, short_filter, rates, residues, skip):
    width = part.shape[2]
    modes = rates.shape[0]
    proj = part.astype(jnp.bfloat16)
    prior = passed_along(proj[:, tok_rows - (TAPS - 1) :, :], "seq", 1)
    padded = jnp.concatenate([prior, proj], axis=1).astype(jnp.float32)
    mixed = jnp.zeros((3, tok_rows, width), jnp.float32)
    for j in range(TAPS):
        mixed = (
            mixed
            + short_filter[:, j, None, :] * padded[:, TAPS - 1 - j : TAPS - 1 - j + tok_rows, :]
        )
    query, key, value = (mixed[0], mixed[1], mixed[2])
    drive = key * value
    position = jnp.arange(tok_rows, dtype=jnp.float32)
    scaled = residues * jnp.sqrt(1.0 - jnp.exp(-2.0 * rates))
    end_powers = jnp.exp(-rates[None, :, :] * (tok_rows - 1.0 - position)[:, None, None])
    end_state = jnp.sum(end_powers * drive[:, None, :], axis=0)
    block_decay = jnp.exp(-rates * tok_rows)
    entering = carried_in(end_state, block_decay, "seq")
    start_powers = jnp.exp(-rates[None, :, :] * (position + 1.0)[:, None, None])
    cross = jnp.sum(start_powers * (scaled * entering)[None, :, :], axis=1)
    center = (tok_rows - 1.0) / 2.0
    offset = (position - center)[:, None, None]
    rising = jnp.exp(rates[None, :, :] * offset) * drive[:, None, :]
    offsets = jnp.arange(tok_rows, dtype=jnp.int32)
    lower = (offsets[:, None] >= offsets[None, :]).astype(jnp.float32)
    prefix = jnp.dot(
        lower, rising.reshape(tok_rows, modes * width), precision=lax.Precision.HIGHEST
    )
    prefix = prefix.reshape(tok_rows, modes, width)
    falling = jnp.exp(-rates[None, :, :] * offset) * scaled[None, :, :]
    local = jnp.sum(falling * prefix, axis=1)
    return (query * (local + cross + skip[None, :] * drive)).astype(jnp.bfloat16)


def solution(mesh):
    in_specs = (
        P("seq", "ch"),
        P(None, "seq", "ch"),
        P(None, None, "ch"),
        P(None, "ch"),
        P(None, "ch"),
        P("ch"),
    )
    out_specs = P("seq", "ch")
    return jax.shard_map(
        per_device, mesh=mesh, in_specs=in_specs, out_specs=out_specs, check_vma=False
    )
```

```python
import jax
import jax.numpy as jnp
from jax import lax
from jax.sharding import PartitionSpec as P

TAPS = 3
CHUNKS = 2
HALO_ROWS = 8


def passed_along(block, axis, distance):
    devices = range(lax.axis_size(axis))
    route = [(i - distance, i) for i in devices if i - distance in devices]
    return lax.ppermute(block, axis, route)


def carried_in(end_state, decay, axis):
    total = lax.axis_size(axis)
    state = jnp.zeros_like(end_state)
    for distance in range(total - 1, 0, -1):
        state = state * decay + passed_along(end_state, axis, distance)
    return state


def gather_block(inputs):
    tok_rows, local = inputs.shape
    n_seq = lax.axis_size("seq")
    n_ch = lax.axis_size("ch")
    share = tok_rows // n_ch
    pieces = lax.all_to_all(inputs.reshape(n_ch, share, local), "ch", 0, 0, tiled=True)
    pieces = pieces.transpose(1, 0, 2).reshape(share, n_seq, (n_ch * local) // n_seq)
    rows = lax.all_to_all(pieces, "seq", 1, 0, tiled=True)
    rows = rows.reshape(n_seq, share, rows.shape[-1])
    block = lax.all_gather(rows, "ch", axis=1, tiled=True)
    halo = TAPS - 1
    before = jnp.concatenate(
        [jnp.zeros_like(block[:1, :halo]), block[:-1, tok_rows - halo :]], axis=0
    )
    pad = jnp.zeros_like(block[:, : HALO_ROWS - halo])
    block = jnp.concatenate([pad, before, block], axis=1)
    return block.reshape(n_seq * (tok_rows + HALO_ROWS), block.shape[-1])


def project(block, w_in):
    partial = jnp.einsum("td,kdc->ktc", block, w_in, preferred_element_type=jnp.float32)
    return lax.psum_scatter(partial, "seq", scatter_dimension=1, tiled=True)


def per_device(inputs, w_in, short_filter, rates, residues, skip):
    block = gather_block(inputs)
    width = w_in.shape[2]
    chunks = max(1, min(CHUNKS, width // 128))
    step = width // chunks
    parts = [project(block, w_in[:, :, i * step : (i + 1) * step]) for i in range(chunks)]
    outs = []
    for i in range(chunks):
        cols = slice(i * step, (i + 1) * step)
        part = parts[i]
        if outs:
            outs[-1], part = lax.optimization_barrier((outs[-1], part))
        outs.append(
            chunk(part, inputs.shape[0], short_filter[:, :, cols],
                  rates[:, cols], residues[:, cols], skip[cols])
        )
    return jnp.concatenate(outs, axis=1)


def chunk(part, tok_rows, short_filter, rates, residues, skip):
    width = part.shape[2]
    modes = rates.shape[0]
    padded = part[:, HALO_ROWS - (TAPS - 1) :].astype(jnp.bfloat16).astype(jnp.float32)
    mixed = jnp.zeros((3, tok_rows, width), jnp.float32)
    for j in range(TAPS):
        mixed = (
            mixed
            + short_filter[:, j, None, :] * padded[:, TAPS - 1 - j : TAPS - 1 - j + tok_rows, :]
        )
    query, key, value = (mixed[0], mixed[1], mixed[2])
    drive = key * value
    position = jnp.arange(tok_rows, dtype=jnp.float32)
    scaled = residues * jnp.sqrt(1.0 - jnp.exp(-2.0 * rates))
    end_powers = jnp.exp(-rates[None, :, :] * (tok_rows - 1.0 - position)[:, None, None])
    end_state = jnp.sum(end_powers * drive[:, None, :], axis=0)
    block_decay = jnp.exp(-rates * tok_rows)
    entering = carried_in(end_state, block_decay, "seq")
    start_powers = jnp.exp(-rates[None, :, :] * (position + 1.0)[:, None, None])
    cross = jnp.sum(start_powers * (scaled * entering)[None, :, :], axis=1)
    center = (tok_rows - 1.0) / 2.0
    offset = (position - center)[:, None, None]
    rising = jnp.exp(rates[None, :, :] * offset) * drive[:, None, :]
    offsets = jnp.arange(tok_rows, dtype=jnp.int32)
    lower = (offsets[:, None] >= offsets[None, :]).astype(jnp.float32)
    prefix = jnp.dot(
        lower, rising.reshape(tok_rows, modes * width), precision=lax.Precision.HIGHEST
    )
    prefix = prefix.reshape(tok_rows, modes, width)
    falling = jnp.exp(-rates[None, :, :] * offset) * scaled[None, :, :]
    local = jnp.sum(falling * prefix, axis=1)
    return (query * (local + cross + skip[None, :] * drive)).astype(jnp.bfloat16)


def solution(mesh):
    in_specs = (
        P("seq", "ch"),
        P(None, "seq", "ch"),
        P(None, None, "ch"),
        P(None, "ch"),
        P(None, "ch"),
        P("ch"),
    )
    out_specs = P("seq", "ch")
    return jax.shard_map(
        per_device, mesh=mesh, in_specs=in_specs, out_specs=out_specs, check_vma=False
    )
```

```python
import jax
import jax.numpy as jnp
from jax import lax
from jax.sharding import PartitionSpec as P

TAPS = 3
CHUNKS = 2


def passed_along(block, axis, distance):
    devices = range(lax.axis_size(axis))
    route = [(i - distance, i) for i in devices if i - distance in devices]
    return lax.ppermute(block, axis, route)


def carried_in(end_state, decay, axis):
    total = lax.axis_size(axis)
    state = jnp.zeros_like(end_state)
    for distance in range(total - 1, 0, -1):
        state = state * decay + passed_along(end_state, axis, distance)
    return state


def gather_block(inputs):
    tok_rows, local = inputs.shape
    n_seq = lax.axis_size("seq")
    n_ch = lax.axis_size("ch")
    share = tok_rows // n_ch
    pieces = lax.all_to_all(inputs.reshape(share, n_ch, local), "ch", 1, 1, tiled=True)
    pieces = pieces.reshape(share, n_seq, (n_ch * local) // n_seq)
    rows = lax.all_to_all(pieces, "seq", 1, 0, tiled=True)
    rows = rows.reshape(n_seq, share, rows.shape[-1])
    halo = TAPS - 1
    last = jnp.concatenate([jnp.zeros_like(rows[:1, -1:]), rows[:-1, -1:]], axis=0)
    keep = lax.axis_index("ch") >= n_ch - halo
    extra = jnp.where(keep, last, jnp.zeros_like(last))
    rows = jnp.concatenate([extra, rows], axis=1)
    block = lax.all_gather(rows, "ch", axis=1, tiled=True)
    return block.reshape(n_seq * n_ch * (share + 1), block.shape[-1])


def unpack(part, tok_rows, n_ch):
    share = tok_rows // n_ch
    part = part.reshape(part.shape[0], n_ch, share + 1, part.shape[-1])
    halo = part[:, n_ch - (TAPS - 1) :, 0, :]
    main = part[:, :, 1:, :].transpose(0, 2, 1, 3).reshape(part.shape[0], tok_rows, part.shape[-1])
    return jnp.concatenate([halo, main], axis=1)


def project(block, w_in):
    partial = jnp.einsum("td,kdc->ktc", block, w_in, preferred_element_type=jnp.float32)
    return lax.psum_scatter(partial, "seq", scatter_dimension=1, tiled=True)


def per_device(inputs, w_in, short_filter, rates, residues, skip):
    block = gather_block(inputs)
    width = w_in.shape[2]
    chunks = max(1, min(CHUNKS, width // 128))
    step = width // chunks
    parts = [project(block, w_in[:, :, i * step : (i + 1) * step]) for i in range(chunks)]
    outs = []
    for i in range(chunks):
        cols = slice(i * step, (i + 1) * step)
        part = parts[i]
        if outs:
            outs[-1], part = lax.optimization_barrier((outs[-1], part))
        outs.append(
            chunk(part, inputs.shape[0], short_filter[:, :, cols],
                  rates[:, cols], residues[:, cols], skip[cols])
        )
    return jnp.concatenate(outs, axis=1)


def chunk(part, tok_rows, short_filter, rates, residues, skip):
    width = part.shape[2]
    modes = rates.shape[0]
    padded = unpack(part, tok_rows, lax.axis_size("ch"))
    padded = lax.reduce_precision(padded, exponent_bits=8, mantissa_bits=7)
    mixed = jnp.zeros((3, tok_rows, width), jnp.float32)
    for j in range(TAPS):
        mixed = (
            mixed
            + short_filter[:, j, None, :] * padded[:, TAPS - 1 - j : TAPS - 1 - j + tok_rows, :]
        )
    query, key, value = (mixed[0], mixed[1], mixed[2])
    drive = key * value
    position = jnp.arange(tok_rows, dtype=jnp.float32)
    scaled = residues * jnp.sqrt(1.0 - jnp.exp(-2.0 * rates))
    end_powers = jnp.exp(-rates[None, :, :] * (tok_rows - 1.0 - position)[:, None, None])
    end_state = jnp.sum(end_powers * drive[:, None, :], axis=0)
    block_decay = jnp.exp(-rates * tok_rows)
    entering = carried_in(end_state, block_decay, "seq")
    start_powers = jnp.exp(-rates[None, :, :] * (position + 1.0)[:, None, None])
    cross = jnp.sum(start_powers * (scaled * entering)[None, :, :], axis=1)
    center = (tok_rows - 1.0) / 2.0
    offset = (position - center)[:, None, None]
    rising = jnp.exp(rates[None, :, :] * offset) * drive[:, None, :]
    offsets = jnp.arange(tok_rows, dtype=jnp.int32)
    lower = (offsets[:, None] >= offsets[None, :]).astype(jnp.float32)
    prefix = jnp.dot(
        lower, rising.reshape(tok_rows, modes * width), precision=lax.Precision.HIGHEST
    )
    prefix = prefix.reshape(tok_rows, modes, width)
    falling = jnp.exp(-rates[None, :, :] * offset) * scaled[None, :, :]
    local = jnp.sum(falling * prefix, axis=1)
    return (query * (local + cross + skip[None, :] * drive)).astype(jnp.bfloat16)


def solution(mesh):
    in_specs = (
        P("seq", "ch"),
        P(None, "seq", "ch"),
        P(None, None, "ch"),
        P(None, "ch"),
        P(None, "ch"),
        P("ch"),
    )
    out_specs = P("seq", "ch")
    return jax.shard_map(
        per_device, mesh=mesh, in_specs=in_specs, out_specs=out_specs, check_vma=False
    )
```

```python
import jax
import jax.numpy as jnp
from jax import lax
from jax.sharding import PartitionSpec as P

TAPS = 3
CHUNKS = 2
HALO_ROWS = 8


def passed_along(block, axis, distance):
    devices = range(lax.axis_size(axis))
    route = [(i - distance, i) for i in devices if i - distance in devices]
    return lax.ppermute(block, axis, route)


def carried_in(end_state, decay, axis):
    total = lax.axis_size(axis)
    state = jnp.zeros_like(end_state)
    for distance in range(total - 1, 0, -1):
        state = state * decay + passed_along(end_state, axis, distance)
    return state


def gather_block(inputs):
    tok_rows, local = inputs.shape
    n_seq = lax.axis_size("seq")
    n_ch = lax.axis_size("ch")
    ratio = n_ch // n_seq
    main, ahead = [], []
    for src_s in range(n_seq):
        for src_c in range(n_ch):
            dst = (src_c // ratio) * n_ch + ratio * src_s + src_c % ratio
            main.append((src_s * n_ch + src_c, dst))
            if src_s + 1 < n_seq:
                ahead.append((src_s * n_ch + src_c, dst + ratio))
    share = lax.ppermute(inputs, ("seq", "ch"), main)
    tail = inputs[tok_rows - HALO_ROWS :]
    tail = jnp.where(jnp.arange(HALO_ROWS)[:, None] >= HALO_ROWS - (TAPS - 1), tail, 0)
    halo = lax.ppermute(tail.astype(inputs.dtype), ("seq", "ch"), ahead)
    piece = jnp.concatenate([halo, share], axis=0)
    block = lax.all_gather(piece, "ch", axis=0, tiled=False)
    return block.reshape(n_seq, ratio, tok_rows + HALO_ROWS, local)


def project(block, w_in):
    ratio, local = block.shape[1], block.shape[3]
    w = w_in.reshape(w_in.shape[0], ratio, local, w_in.shape[2])
    partial = jnp.einsum("serk,xekc->xsrc", block, w, preferred_element_type=jnp.float32)
    partial = partial.reshape(partial.shape[0], -1, partial.shape[-1])
    return lax.psum_scatter(partial, "seq", scatter_dimension=1, tiled=True)


def per_device(inputs, w_in, short_filter, rates, residues, skip):
    block = gather_block(inputs)
    width = w_in.shape[2]
    chunks = max(1, min(CHUNKS, width // 128))
    step = width // chunks
    parts = [project(block, w_in[:, :, i * step : (i + 1) * step]) for i in range(chunks)]
    outs = []
    for i in range(chunks):
        cols = slice(i * step, (i + 1) * step)
        part = parts[i]
        if outs:
            outs[-1], part = lax.optimization_barrier((outs[-1], part))
        outs.append(
            chunk(part, inputs.shape[0], short_filter[:, :, cols],
                  rates[:, cols], residues[:, cols], skip[cols])
        )
    return jnp.concatenate(outs, axis=1)


def chunk(part, tok_rows, short_filter, rates, residues, skip):
    width = part.shape[2]
    modes = rates.shape[0]
    padded = part[:, HALO_ROWS - (TAPS - 1) :]
    padded = lax.reduce_precision(padded, exponent_bits=8, mantissa_bits=7)
    mixed = jnp.zeros((3, tok_rows, width), jnp.float32)
    for j in range(TAPS):
        mixed = (
            mixed
            + short_filter[:, j, None, :] * padded[:, TAPS - 1 - j : TAPS - 1 - j + tok_rows, :]
        )
    query, key, value = (mixed[0], mixed[1], mixed[2])
    drive = key * value
    position = jnp.arange(tok_rows, dtype=jnp.float32)
    scaled = residues * jnp.sqrt(1.0 - jnp.exp(-2.0 * rates))
    end_powers = jnp.exp(-rates[None, :, :] * (tok_rows - 1.0 - position)[:, None, None])
    end_state = jnp.sum(end_powers * drive[:, None, :], axis=0)
    block_decay = jnp.exp(-rates * tok_rows)
    entering = carried_in(end_state, block_decay, "seq")
    start_powers = jnp.exp(-rates[None, :, :] * (position + 1.0)[:, None, None])
    cross = jnp.sum(start_powers * (scaled * entering)[None, :, :], axis=1)
    center = (tok_rows - 1.0) / 2.0
    offset = (position - center)[:, None, None]
    rising = jnp.exp(rates[None, :, :] * offset) * drive[:, None, :]
    offsets = jnp.arange(tok_rows, dtype=jnp.int32)
    lower = (offsets[:, None] >= offsets[None, :]).astype(jnp.float32)
    prefix = jnp.dot(
        lower, rising.reshape(tok_rows, modes * width), precision=lax.Precision.HIGHEST
    )
    prefix = prefix.reshape(tok_rows, modes, width)
    falling = jnp.exp(-rates[None, :, :] * offset) * scaled[None, :, :]
    local = jnp.sum(falling * prefix, axis=1)
    return (query * (local + cross + skip[None, :] * drive)).astype(jnp.bfloat16)


def solution(mesh):
    in_specs = (
        P("seq", "ch"),
        P(None, "seq", "ch"),
        P(None, None, "ch"),
        P(None, "ch"),
        P(None, "ch"),
        P("ch"),
    )
    out_specs = P("seq", "ch")
    return jax.shard_map(
        per_device, mesh=mesh, in_specs=in_specs, out_specs=out_specs, check_vma=False
    )
```

```python
import jax
import jax.numpy as jnp
from jax import lax
from jax.sharding import PartitionSpec as P

TAPS = 3


def passed_along(block, axis, distance):
    devices = range(lax.axis_size(axis))
    route = [(i - distance, i) for i in devices if i - distance in devices]
    return lax.ppermute(block, axis, route)


def carried_in(end_state, decay, axis):
    total = lax.axis_size(axis)
    state = jnp.zeros_like(end_state)
    for distance in range(total - 1, 0, -1):
        state = state * decay + passed_along(end_state, axis, distance)
    return state


def gather_block(inputs):
    tok_rows, local = inputs.shape
    n_seq = lax.axis_size("seq")
    n_ch = lax.axis_size("ch")
    share = tok_rows // n_ch
    pieces = lax.all_to_all(inputs.reshape(share, n_ch, local), "ch", 1, 1, tiled=True)
    pieces = pieces.reshape(share, n_seq, (n_ch * local) // n_seq)
    rows = lax.all_to_all(pieces, "seq", 1, 0, tiled=True)
    rows = rows.reshape(n_seq, share, rows.shape[-1])
    halo = TAPS - 1
    last = jnp.concatenate([jnp.zeros_like(rows[:1, -1:]), rows[:-1, -1:]], axis=0)
    keep = lax.axis_index("ch") >= n_ch - halo
    extra = jnp.where(keep, last, jnp.zeros_like(last))
    rows = jnp.concatenate([extra, rows], axis=1)
    block = lax.all_gather(rows, "ch", axis=1, tiled=True)
    return block.reshape(n_seq * n_ch * (share + 1), block.shape[-1])


def unpack(part, tok_rows, n_ch):
    share = tok_rows // n_ch
    part = part.reshape(part.shape[0], n_ch, share + 1, part.shape[-1])
    halo = part[:, n_ch - (TAPS - 1) :, 0, :]
    main = part[:, :, 1:, :].transpose(0, 2, 1, 3).reshape(part.shape[0], tok_rows, part.shape[-1])
    return jnp.concatenate([halo, main], axis=1)


def project(block, w_in):
    partial = jnp.einsum("td,kdc->ktc", block, w_in, preferred_element_type=jnp.float32)
    return lax.psum_scatter(partial, "seq", scatter_dimension=1, tiled=True)


def per_device(inputs, w_in, short_filter, rates, residues, skip):
    tok_rows = inputs.shape[0]
    n_ch = lax.axis_size("ch")
    block = gather_block(inputs)
    pair = project(block, w_in[1:])
    single = project(block, w_in[:1])
    key, value = short_conv(unpack(pair, tok_rows, n_ch), short_filter[1:], tok_rows)
    drive = key * value
    mixed = long_conv(drive, tok_rows, rates, residues, skip)
    mixed, single = lax.optimization_barrier((mixed, single))
    query = short_conv(unpack(single, tok_rows, n_ch), short_filter[:1], tok_rows)[0]
    return (query * mixed).astype(jnp.bfloat16)


def short_conv(part, short_filter, tok_rows):
    padded = lax.reduce_precision(part, exponent_bits=8, mantissa_bits=7)
    mixed = jnp.zeros((part.shape[0], tok_rows, part.shape[2]), jnp.float32)
    for j in range(TAPS):
        mixed = (
            mixed
            + short_filter[:, j, None, :] * padded[:, TAPS - 1 - j : TAPS - 1 - j + tok_rows, :]
        )
    return mixed


def long_conv(drive, tok_rows, rates, residues, skip):
    width = drive.shape[1]
    modes = rates.shape[0]
    position = jnp.arange(tok_rows, dtype=jnp.float32)
    scaled = residues * jnp.sqrt(1.0 - jnp.exp(-2.0 * rates))
    end_powers = jnp.exp(-rates[None, :, :] * (tok_rows - 1.0 - position)[:, None, None])
    end_state = jnp.sum(end_powers * drive[:, None, :], axis=0)
    block_decay = jnp.exp(-rates * tok_rows)
    entering = carried_in(end_state, block_decay, "seq")
    start_powers = jnp.exp(-rates[None, :, :] * (position + 1.0)[:, None, None])
    cross = jnp.sum(start_powers * (scaled * entering)[None, :, :], axis=1)
    center = (tok_rows - 1.0) / 2.0
    offset = (position - center)[:, None, None]
    rising = jnp.exp(rates[None, :, :] * offset) * drive[:, None, :]
    offsets = jnp.arange(tok_rows, dtype=jnp.int32)
    lower = (offsets[:, None] >= offsets[None, :]).astype(jnp.float32)
    prefix = jnp.dot(
        lower, rising.reshape(tok_rows, modes * width), precision=lax.Precision.HIGHEST
    )
    prefix = prefix.reshape(tok_rows, modes, width)
    falling = jnp.exp(-rates[None, :, :] * offset) * scaled[None, :, :]
    local = jnp.sum(falling * prefix, axis=1)
    return local + cross + skip[None, :] * drive


def solution(mesh):
    in_specs = (
        P("seq", "ch"),
        P(None, "seq", "ch"),
        P(None, None, "ch"),
        P(None, "ch"),
        P(None, "ch"),
        P("ch"),
    )
    out_specs = P("seq", "ch")
    return jax.shard_map(
        per_device, mesh=mesh, in_specs=in_specs, out_specs=out_specs, check_vma=False
    )
```

```python
import jax
import jax.numpy as jnp
from jax import lax
from jax.sharding import PartitionSpec as P

TAPS = 3
HALO_ROWS = 8


def passed_along(block, axis, distance):
    devices = range(lax.axis_size(axis))
    route = [(i - distance, i) for i in devices if i - distance in devices]
    return lax.ppermute(block, axis, route)


def carried_in(end_state, decay, axis):
    total = lax.axis_size(axis)
    state = jnp.zeros_like(end_state)
    for distance in range(total - 1, 0, -1):
        state = state * decay + passed_along(end_state, axis, distance)
    return state


def gather_block(inputs):
    tok_rows, local = inputs.shape
    n_seq = lax.axis_size("seq")
    n_ch = lax.axis_size("ch")
    ratio = n_ch // n_seq
    main, ahead = [], []
    for src_s in range(n_seq):
        for src_c in range(n_ch):
            dst = (src_c // ratio) * n_ch + ratio * src_s + src_c % ratio
            main.append((src_s * n_ch + src_c, dst))
            if src_s + 1 < n_seq:
                ahead.append((src_s * n_ch + src_c, dst + ratio))
    share = lax.ppermute(inputs, ("seq", "ch"), main)
    tail = inputs[tok_rows - HALO_ROWS :]
    tail = jnp.where(jnp.arange(HALO_ROWS)[:, None] >= HALO_ROWS - (TAPS - 1), tail, 0)
    halo = lax.ppermute(tail.astype(inputs.dtype), ("seq", "ch"), ahead)
    piece = jnp.concatenate([halo, share], axis=0)
    block = lax.all_gather(piece, "ch", axis=0, tiled=False)
    return block.reshape(n_seq, ratio, tok_rows + HALO_ROWS, local)


def project(block, w_in):
    ratio, local = block.shape[1], block.shape[3]
    w = w_in.reshape(w_in.shape[0], ratio, local, w_in.shape[2])
    partial = jnp.einsum("serk,xekc->srxc", block, w, preferred_element_type=jnp.float32)
    partial = partial.reshape(-1, partial.shape[2], partial.shape[3])
    part = lax.psum_scatter(partial, "seq", scatter_dimension=0, tiled=True)
    return jnp.moveaxis(part[HALO_ROWS - (TAPS - 1) :], 1, 0)


def per_device(inputs, w_in, short_filter, rates, residues, skip):
    tok_rows = inputs.shape[0]
    block = gather_block(inputs)
    pair = project(block, w_in[1:])
    single = project(block, w_in[:1])
    key, value = short_conv(pair, short_filter[1:], tok_rows)
    drive = key * value
    mixed = long_conv(drive, tok_rows, rates, residues, skip)
    mixed, single = lax.optimization_barrier((mixed, single))
    query = short_conv(single, short_filter[:1], tok_rows)[0]
    return (query * mixed).astype(jnp.bfloat16)


def short_conv(part, short_filter, tok_rows):
    padded = lax.reduce_precision(part, exponent_bits=8, mantissa_bits=7)
    mixed = jnp.zeros((part.shape[0], tok_rows, part.shape[2]), jnp.float32)
    for j in range(TAPS):
        mixed = (
            mixed
            + short_filter[:, j, None, :] * padded[:, TAPS - 1 - j : TAPS - 1 - j + tok_rows, :]
        )
    return mixed


def long_conv(drive, tok_rows, rates, residues, skip):
    width = drive.shape[1]
    modes = rates.shape[0]
    position = jnp.arange(tok_rows, dtype=jnp.float32)
    scaled = residues * jnp.sqrt(1.0 - jnp.exp(-2.0 * rates))
    end_powers = jnp.exp(-rates[None, :, :] * (tok_rows - 1.0 - position)[:, None, None])
    end_state = jnp.sum(end_powers * drive[:, None, :], axis=0)
    block_decay = jnp.exp(-rates * tok_rows)
    entering = carried_in(end_state, block_decay, "seq")
    start_powers = jnp.exp(-rates[None, :, :] * (position + 1.0)[:, None, None])
    cross = jnp.sum(start_powers * (scaled * entering)[None, :, :], axis=1)
    center = (tok_rows - 1.0) / 2.0
    offset = (position - center)[:, None, None]
    rising = jnp.exp(rates[None, :, :] * offset) * drive[:, None, :]
    offsets = jnp.arange(tok_rows, dtype=jnp.int32)
    lower = (offsets[:, None] >= offsets[None, :]).astype(jnp.float32)
    prefix = jnp.dot(
        lower, rising.reshape(tok_rows, modes * width), precision=lax.Precision.HIGHEST
    )
    prefix = prefix.reshape(tok_rows, modes, width)
    falling = jnp.exp(-rates[None, :, :] * offset) * scaled[None, :, :]
    local = jnp.sum(falling * prefix, axis=1)
    return local + cross + skip[None, :] * drive


def solution(mesh):
    in_specs = (
        P("seq", "ch"),
        P(None, "seq", "ch"),
        P(None, None, "ch"),
        P(None, "ch"),
        P(None, "ch"),
        P("ch"),
    )
    out_specs = P("seq", "ch")
    return jax.shard_map(
        per_device, mesh=mesh, in_specs=in_specs, out_specs=out_specs, check_vma=False
    )
```

```python
import jax
import jax.numpy as jnp
from jax import lax
from jax.sharding import Mesh, PartitionSpec as P

TAPS = 3
CH = ("chip", "core")


def passed_along(block, axis, distance):
    devices = range(lax.axis_size(axis))
    route = [(i - distance, i) for i in devices if i - distance in devices]
    return lax.ppermute(block, axis, route)


def carried_in(end_state, decay, axis):
    total = lax.axis_size(axis)
    state = jnp.zeros_like(end_state)
    for distance in range(total - 1, 0, -1):
        state = state * decay + passed_along(end_state, axis, distance)
    return state


def gather_block(inputs):
    tok_rows, local = inputs.shape
    n_seq = lax.axis_size("seq")
    n_ch = lax.axis_size(CH)
    share = tok_rows // n_ch
    pieces = lax.all_to_all(inputs.reshape(share, n_ch, local), CH, 1, 1, tiled=True)
    pieces = pieces.reshape(share, n_seq, (n_ch * local) // n_seq)
    rows = lax.all_to_all(pieces, "seq", 1, 0, tiled=True)
    rows = rows.reshape(n_seq, share, rows.shape[-1])
    halo = TAPS - 1
    last = jnp.concatenate([jnp.zeros_like(rows[:1, -1:]), rows[:-1, -1:]], axis=0)
    keep = lax.axis_index(CH) >= n_ch - halo
    extra = jnp.where(keep, last, jnp.zeros_like(last))
    rows = jnp.concatenate([extra, rows], axis=1)
    block = lax.all_gather(rows, "chip", axis=1, tiled=True)
    block = lax.all_gather(block, "core", axis=1, tiled=True)
    return block.reshape(n_seq * n_ch * (share + 1), block.shape[-1])


def unpack(part, tok_rows, n_ch):
    share = tok_rows // n_ch
    cores = lax.axis_size("core")
    part = part.reshape(part.shape[0], cores, n_ch // cores, share + 1, part.shape[-1])
    part = part.transpose(0, 2, 1, 3, 4).reshape(part.shape[0], n_ch, share + 1, part.shape[-1])
    halo = part[:, n_ch - (TAPS - 1) :, 0, :]
    main = part[:, :, 1:, :].transpose(0, 2, 1, 3).reshape(part.shape[0], tok_rows, part.shape[-1])
    return jnp.concatenate([halo, main], axis=1)


def project(block, w_in):
    partial = jnp.einsum("td,kdc->ktc", block, w_in, preferred_element_type=jnp.float32)
    return lax.psum_scatter(partial, "seq", scatter_dimension=1, tiled=True)


def per_device(inputs, w_in, short_filter, rates, residues, skip):
    tok_rows = inputs.shape[0]
    n_ch = lax.axis_size(CH)
    block = gather_block(inputs)
    pair = project(block, w_in[1:])
    single = project(block, w_in[:1])
    key, value = short_conv(unpack(pair, tok_rows, n_ch), short_filter[1:], tok_rows)
    drive = key * value
    mixed = long_conv(drive, tok_rows, rates, residues, skip)
    mixed, single = lax.optimization_barrier((mixed, single))
    query = short_conv(unpack(single, tok_rows, n_ch), short_filter[:1], tok_rows)[0]
    return (query * mixed).astype(jnp.bfloat16)


def short_conv(part, short_filter, tok_rows):
    padded = lax.reduce_precision(part, exponent_bits=8, mantissa_bits=7)
    mixed = jnp.zeros((part.shape[0], tok_rows, part.shape[2]), jnp.float32)
    for j in range(TAPS):
        mixed = (
            mixed
            + short_filter[:, j, None, :] * padded[:, TAPS - 1 - j : TAPS - 1 - j + tok_rows, :]
        )
    return mixed


def long_conv(drive, tok_rows, rates, residues, skip):
    width = drive.shape[1]
    modes = rates.shape[0]
    position = jnp.arange(tok_rows, dtype=jnp.float32)
    scaled = residues * jnp.sqrt(1.0 - jnp.exp(-2.0 * rates))
    end_powers = jnp.exp(-rates[None, :, :] * (tok_rows - 1.0 - position)[:, None, None])
    end_state = jnp.sum(end_powers * drive[:, None, :], axis=0)
    block_decay = jnp.exp(-rates * tok_rows)
    entering = carried_in(end_state, block_decay, "seq")
    start_powers = jnp.exp(-rates[None, :, :] * (position + 1.0)[:, None, None])
    cross = jnp.sum(start_powers * (scaled * entering)[None, :, :], axis=1)
    center = (tok_rows - 1.0) / 2.0
    offset = (position - center)[:, None, None]
    rising = jnp.exp(rates[None, :, :] * offset) * drive[:, None, :]
    offsets = jnp.arange(tok_rows, dtype=jnp.int32)
    lower = (offsets[:, None] >= offsets[None, :]).astype(jnp.float32)
    prefix = jnp.dot(
        lower, rising.reshape(tok_rows, modes * width), precision=lax.Precision.HIGHEST
    )
    prefix = prefix.reshape(tok_rows, modes, width)
    falling = jnp.exp(-rates[None, :, :] * offset) * scaled[None, :, :]
    local = jnp.sum(falling * prefix, axis=1)
    return local + cross + skip[None, :] * drive


def solution(mesh):
    seq, ch = mesh.devices.shape
    mesh = Mesh(mesh.devices.reshape(seq, ch // 2, 2), ("seq", "chip", "core"))
    in_specs = (
        P("seq", CH),
        P(None, "seq", CH),
        P(None, None, CH),
        P(None, CH),
        P(None, CH),
        P(CH),
    )
    out_specs = P("seq", CH)
    return jax.shard_map(
        per_device, mesh=mesh, in_specs=in_specs, out_specs=out_specs, check_vma=False
    )
```

```python
import jax
import jax.numpy as jnp
from jax import lax
from jax.sharding import PartitionSpec as P

TAPS = 3


def passed_along(block, axis, distance):
    devices = range(lax.axis_size(axis))
    route = [(i - distance, i) for i in devices if i - distance in devices]
    return lax.ppermute(block, axis, route)


def carried_in(end_state, decay, axis):
    total = lax.axis_size(axis)
    state = jnp.zeros_like(end_state)
    for distance in range(total - 1, 0, -1):
        state = state * decay + passed_along(end_state, axis, distance)
    return state


def gather_block(inputs):
    tok_rows, local = inputs.shape
    n_seq = lax.axis_size("seq")
    n_ch = lax.axis_size("ch")
    share = tok_rows // n_ch
    pieces = lax.all_to_all(inputs.reshape(share, n_ch, local), "ch", 1, 1, tiled=True)
    pieces = pieces.reshape(share, n_seq, (n_ch * local) // n_seq)
    rows = spread(pieces, "seq")
    halo = TAPS - 1
    last = jnp.concatenate([jnp.zeros_like(rows[:1, -1:]), rows[:-1, -1:]], axis=0)
    keep = lax.axis_index("ch") >= n_ch - halo
    extra = jnp.where(keep, last, jnp.zeros_like(last))
    rows = jnp.concatenate([extra, rows], axis=1)
    block = lax.all_gather(rows, "ch", axis=1, tiled=True)
    return block.reshape(n_seq * n_ch * (share + 1), block.shape[-1])


def spread(pieces, axis):
    total = lax.axis_size(axis)
    place = lax.axis_index(axis)
    got = [lax.dynamic_index_in_dim(pieces, place, 1, False)]
    for distance in range(1, total):
        out = lax.dynamic_index_in_dim(pieces, (place + distance) % total, 1, False)
        route = [(i, (i + distance) % total) for i in range(total)]
        got.append(lax.ppermute(out, axis, route))
    got = jnp.stack(got)
    return jnp.take(got, (place - jnp.arange(total)) % total, axis=0)


def unpack(part, tok_rows, n_ch):
    share = tok_rows // n_ch
    part = part.reshape(part.shape[0], n_ch, share + 1, part.shape[-1])
    halo = part[:, n_ch - (TAPS - 1) :, 0, :]
    main = part[:, :, 1:, :].transpose(0, 2, 1, 3).reshape(part.shape[0], tok_rows, part.shape[-1])
    return jnp.concatenate([halo, main], axis=1)


def project(block, w_in):
    partial = jnp.einsum("td,kdc->ktc", block, w_in, preferred_element_type=jnp.float32)
    return lax.psum_scatter(partial, "seq", scatter_dimension=1, tiled=True)


def per_device(inputs, w_in, short_filter, rates, residues, skip):
    tok_rows = inputs.shape[0]
    n_ch = lax.axis_size("ch")
    block = gather_block(inputs)
    pair = project(block, w_in[1:])
    single = project(block, w_in[:1])
    key, value = short_conv(unpack(pair, tok_rows, n_ch), short_filter[1:], tok_rows)
    drive = key * value
    mixed = long_conv(drive, tok_rows, rates, residues, skip)
    mixed, single = lax.optimization_barrier((mixed, single))
    query = short_conv(unpack(single, tok_rows, n_ch), short_filter[:1], tok_rows)[0]
    return (query * mixed).astype(jnp.bfloat16)


def short_conv(part, short_filter, tok_rows):
    padded = lax.reduce_precision(part, exponent_bits=8, mantissa_bits=7)
    mixed = jnp.zeros((part.shape[0], tok_rows, part.shape[2]), jnp.float32)
    for j in range(TAPS):
        mixed = (
            mixed
            + short_filter[:, j, None, :] * padded[:, TAPS - 1 - j : TAPS - 1 - j + tok_rows, :]
        )
    return mixed


def long_conv(drive, tok_rows, rates, residues, skip):
    width = drive.shape[1]
    modes = rates.shape[0]
    position = jnp.arange(tok_rows, dtype=jnp.float32)
    scaled = residues * jnp.sqrt(1.0 - jnp.exp(-2.0 * rates))
    end_powers = jnp.exp(-rates[None, :, :] * (tok_rows - 1.0 - position)[:, None, None])
    end_state = jnp.sum(end_powers * drive[:, None, :], axis=0)
    block_decay = jnp.exp(-rates * tok_rows)
    entering = carried_in(end_state, block_decay, "seq")
    start_powers = jnp.exp(-rates[None, :, :] * (position + 1.0)[:, None, None])
    cross = jnp.sum(start_powers * (scaled * entering)[None, :, :], axis=1)
    center = (tok_rows - 1.0) / 2.0
    offset = (position - center)[:, None, None]
    rising = jnp.exp(rates[None, :, :] * offset) * drive[:, None, :]
    offsets = jnp.arange(tok_rows, dtype=jnp.int32)
    lower = (offsets[:, None] >= offsets[None, :]).astype(jnp.float32)
    prefix = jnp.dot(
        lower, rising.reshape(tok_rows, modes * width), precision=lax.Precision.HIGHEST
    )
    prefix = prefix.reshape(tok_rows, modes, width)
    falling = jnp.exp(-rates[None, :, :] * offset) * scaled[None, :, :]
    local = jnp.sum(falling * prefix, axis=1)
    return local + cross + skip[None, :] * drive


def solution(mesh):
    in_specs = (
        P("seq", "ch"),
        P(None, "seq", "ch"),
        P(None, None, "ch"),
        P(None, "ch"),
        P(None, "ch"),
        P("ch"),
    )
    out_specs = P("seq", "ch")
    return jax.shard_map(
        per_device, mesh=mesh, in_specs=in_specs, out_specs=out_specs, check_vma=False
    )
```

```python
import jax
import jax.numpy as jnp
from jax import lax
from jax.sharding import PartitionSpec as P

TAPS = 3


def passed_along(block, axis, distance):
    devices = range(lax.axis_size(axis))
    route = [(i - distance, i) for i in devices if i - distance in devices]
    return lax.ppermute(block, axis, route)


def carried_in(end_state, decay, axis):
    total = lax.axis_size(axis)
    state = jnp.zeros_like(end_state)
    for distance in range(total - 1, 0, -1):
        state = state * decay + passed_along(end_state, axis, distance)
    return state


def gather_block(inputs):
    tok_rows, local = inputs.shape
    n_seq = lax.axis_size("seq")
    n_ch = lax.axis_size("ch")
    share = tok_rows // n_ch
    pieces = spread(inputs.reshape(share, n_ch, local), "ch").transpose(1, 0, 2)
    pieces = pieces.reshape(share, n_seq, (n_ch * local) // n_seq)
    rows = spread(pieces, "seq")
    halo = TAPS - 1
    last = jnp.concatenate([jnp.zeros_like(rows[:1, -1:]), rows[:-1, -1:]], axis=0)
    keep = lax.axis_index("ch") >= n_ch - halo
    extra = jnp.where(keep, last, jnp.zeros_like(last))
    rows = jnp.concatenate([extra, rows], axis=1)
    block = lax.all_gather(rows, "ch", axis=1, tiled=True)
    return block.reshape(n_seq * n_ch * (share + 1), block.shape[-1])


def spread(pieces, axis):
    total = lax.axis_size(axis)
    place = lax.axis_index(axis)
    got = [lax.dynamic_index_in_dim(pieces, place, 1, False)]
    for distance in range(1, total):
        out = lax.dynamic_index_in_dim(pieces, (place + distance) % total, 1, False)
        route = [(i, (i + distance) % total) for i in range(total)]
        got.append(lax.ppermute(out, axis, route))
    got = jnp.stack(got)
    return jnp.take(got, (place - jnp.arange(total)) % total, axis=0)


def unpack(part, tok_rows, n_ch):
    share = tok_rows // n_ch
    part = part.reshape(part.shape[0], n_ch, share + 1, part.shape[-1])
    halo = part[:, n_ch - (TAPS - 1) :, 0, :]
    main = part[:, :, 1:, :].transpose(0, 2, 1, 3).reshape(part.shape[0], tok_rows, part.shape[-1])
    return jnp.concatenate([halo, main], axis=1)


def project(block, w_in):
    partial = jnp.einsum("td,kdc->ktc", block, w_in, preferred_element_type=jnp.float32)
    return lax.psum_scatter(partial, "seq", scatter_dimension=1, tiled=True)


def per_device(inputs, w_in, short_filter, rates, residues, skip):
    tok_rows = inputs.shape[0]
    n_ch = lax.axis_size("ch")
    block = gather_block(inputs)
    pair = project(block, w_in[1:])
    single = project(block, w_in[:1])
    key, value = short_conv(unpack(pair, tok_rows, n_ch), short_filter[1:], tok_rows)
    drive = key * value
    mixed = long_conv(drive, tok_rows, rates, residues, skip)
    mixed, single = lax.optimization_barrier((mixed, single))
    query = short_conv(unpack(single, tok_rows, n_ch), short_filter[:1], tok_rows)[0]
    return (query * mixed).astype(jnp.bfloat16)


def short_conv(part, short_filter, tok_rows):
    padded = lax.reduce_precision(part, exponent_bits=8, mantissa_bits=7)
    mixed = jnp.zeros((part.shape[0], tok_rows, part.shape[2]), jnp.float32)
    for j in range(TAPS):
        mixed = (
            mixed
            + short_filter[:, j, None, :] * padded[:, TAPS - 1 - j : TAPS - 1 - j + tok_rows, :]
        )
    return mixed


def long_conv(drive, tok_rows, rates, residues, skip):
    width = drive.shape[1]
    modes = rates.shape[0]
    position = jnp.arange(tok_rows, dtype=jnp.float32)
    scaled = residues * jnp.sqrt(1.0 - jnp.exp(-2.0 * rates))
    end_powers = jnp.exp(-rates[None, :, :] * (tok_rows - 1.0 - position)[:, None, None])
    end_state = jnp.sum(end_powers * drive[:, None, :], axis=0)
    block_decay = jnp.exp(-rates * tok_rows)
    entering = carried_in(end_state, block_decay, "seq")
    start_powers = jnp.exp(-rates[None, :, :] * (position + 1.0)[:, None, None])
    cross = jnp.sum(start_powers * (scaled * entering)[None, :, :], axis=1)
    center = (tok_rows - 1.0) / 2.0
    offset = (position - center)[:, None, None]
    rising = jnp.exp(rates[None, :, :] * offset) * drive[:, None, :]
    offsets = jnp.arange(tok_rows, dtype=jnp.int32)
    lower = (offsets[:, None] >= offsets[None, :]).astype(jnp.float32)
    prefix = jnp.dot(
        lower, rising.reshape(tok_rows, modes * width), precision=lax.Precision.HIGHEST
    )
    prefix = prefix.reshape(tok_rows, modes, width)
    falling = jnp.exp(-rates[None, :, :] * offset) * scaled[None, :, :]
    local = jnp.sum(falling * prefix, axis=1)
    return local + cross + skip[None, :] * drive


def solution(mesh):
    in_specs = (
        P("seq", "ch"),
        P(None, "seq", "ch"),
        P(None, None, "ch"),
        P(None, "ch"),
        P(None, "ch"),
        P("ch"),
    )
    out_specs = P("seq", "ch")
    return jax.shard_map(
        per_device, mesh=mesh, in_specs=in_specs, out_specs=out_specs, check_vma=False
    )
```
